32 devices in a mesh: groups: 2 (over y), section: 4 (over x, core), filt: 4 (over z).
Axes of the slice: x: 2, y: 2, z: 4, core: 2. Of those that a mesh axis runs over, the one named last changes fastest.
Arguments:
- volumes: bfloat16 [16, 256, 4, 2, 128], P('groups', 'filt'), parts along dimension 0, may hold values from -6 to 6
- weights: bfloat16 [4, 256, 27, 256], P('section', 'filt'), may hold values from -0.125 to 0.125
- biases: float32 [4, 256], P('section', 'filt'), may hold values from -3 to 3
- cotangent: bfloat16 [16, 256, 4, 2, 128], P('groups', 'filt'), parts along dimension 0, may hold values from -6 to 6
Outputs:
- grad_weights: float32 [8, 256, 27, 256], P(('groups', 'section'), 'filt'), parts along dimension 0
- grad_biases: float32 [8, 256], P(('groups', 'section'), 'filt'), parts along dimension 0
- grad_inputs: bfloat16 [8, 8, 256, 4, 2, 128], P(('groups', 'section'), None, 'filt'), parts along dimension 0
The draws below stay inside these ranges and needn't reach their ends.
There are 2 independent parts, one for each index of `groups`. The reference program is written for one: setup_inputs(seed, part) draws one part's arguments, and reference() takes and returns one part's arrays. A program takes and returns all parts, laid end to end along the dimension named above; an argument that names none is the same for every part. Nothing has to cross between parts.
All inputs are finite; a program needn't handle non-finite values.
Results may differ from the reference program's by a relative error of at most 0.019.
Values may be sent and summed in bfloat16 or wider, within the bound.
No kernel may reach another device: no remote copies, remote signals or barrier semaphores. Data moves between devices by JAX's collectives and lax.ppermute only.
A program may use at most 64 MiB of HBM per device.

```python
import math
import jax
import jax.numpy as jnp
from jax import lax

CHANNELS = 256
MICRO = 8
CX = 4
CY = 2
CZ = 128
LAYERS = 4


def levels(stream_key, extent, cuts, least, high):
    loudness = 1.0
    for position, parts in cuts:
        draws = jax.random.uniform(jax.random.fold_in(jax.random.fold_in(stream_key, 6), position), (parts,), jnp.float32, least / len(cuts), high / len(cuts))
        loudness = loudness * jnp.repeat(jnp.exp(draws), extent[position] // parts).reshape((-1,) + (1,) * (len(extent) - 1 - position))
    return loudness


def scatter_about(own_key, shape, spread, reach, cuts=(), held_as=jnp.bfloat16):
    result = jax.random.normal(own_key, shape, jnp.float32) * spread
    if len(cuts) > 0:
        result = levels(own_key, shape, cuts, -0.22, 0.18) * result
    return jnp.clip(result, min=-reach, max=reach).astype(held_as)


def setup_inputs(seed: int = 0, part: int = 0) -> dict:
    keys = jax.random.split(jax.random.key(seed), 5)
    part_splits = jax.random.split(jax.random.fold_in(keys[4], part), 5)
    volumes = scatter_about(part_splits[0], (MICRO, CHANNELS, CX, CY, CZ), 1.0, 6.0, ((1, 4),))
    weights = scatter_about(keys[1], (LAYERS, CHANNELS, 27, CHANNELS), (9 * CHANNELS) ** -0.5, 0.125, ((0, 4), (1, 4)))
    biases = scatter_about(keys[2], (LAYERS, CHANNELS), 0.5, 3.0, ((0, 4), (1, 4)), jnp.float32)
    cotangent = scatter_about(part_splits[3], (MICRO, CHANNELS, CX, CY, CZ), 1.0, 6.0, ((1, 4),))
    return {"volumes": volumes, "weights": weights, "biases": biases, "cotangent": cotangent}


tap_offsets = [(first, second, third) for first in (-1, 0, 1) for second in (-1, 0, 1) for third in (-1, 0, 1)]

def shift_cells(values, step_first, step_second, step_third):
    leading = values.ndim - 3
    padded = jnp.pad(values, [(0, 0)] * leading + [(1, 1)] * 3)
    extents = values.shape[-3:]
    return padded[..., 1 + step_first:1 + step_first + extents[0], 1 + step_second:1 + step_second + extents[1], 1 + step_third:1 + step_third + extents[2]]

def sum_taps(product, direction):
    summed = jnp.zeros(product.shape[:1] + product.shape[2:], jnp.float32)
    for tap_index, offset in enumerate(tap_offsets):
        summed = summed + shift_cells(product[:, tap_index], direction * offset[0], direction * offset[1], direction * offset[2])
    return summed

def stack_taps(values, direction):
    return jnp.stack([shift_cells(values, direction * offset[0], direction * offset[1], direction * offset[2]) for offset in tap_offsets], axis=1)

def silu_slope(pre_act):
    sigmoid = jax.nn.sigmoid(pre_act)
    return sigmoid * (1.0 + pre_act * (1.0 - sigmoid))

def conv_layer(activation, weight, layer_bias):
    flattened = activation.reshape(activation.shape[0], -1)
    product = jnp.dot(weight.reshape(-1, weight.shape[2]), flattened, preferred_element_type=jnp.float32)
    product = product.reshape((weight.shape[0], weight.shape[1]) + activation.shape[1:])
    return sum_taps(product, 1) + layer_bias[:, None, None, None]

def reference(volumes, weights, biases, cotangent):
    norm_scale = 1.0 / math.sqrt(MICRO * CX * CY * CZ)
    layer_inputs = [volumes]
    layer_pre = []
    for layer_pos in range(LAYERS):
        current = layer_inputs[-1]
        pre_list = [conv_layer(current[sample], weights[layer_pos], biases[layer_pos]) for sample in range(MICRO)]
        layer_pre.append(pre_list)
        layer_inputs.append(jnp.stack([jax.nn.silu(pre_act).astype(jnp.bfloat16) for pre_act in pre_list]))
    upstream = cotangent
    weight_grads = []
    bias_grads = []
    input_grads = []
    for layer_pos in reversed(range(LAYERS)):
        weight_rows = weights[layer_pos].reshape(-1, CHANNELS)
        weight_sum = jnp.zeros((CHANNELS * 27, CHANNELS), jnp.float32)
        bias_sum = jnp.zeros((CHANNELS,), jnp.float32)
        downstream = []
        for sample in range(MICRO):
            slope_grad = (upstream[sample].astype(jnp.float32) * silu_slope(layer_pre[layer_pos][sample])).astype(jnp.bfloat16)
            stacked = stack_taps(slope_grad, -1).reshape(CHANNELS * 27, -1)
            flat_input = layer_inputs[layer_pos][sample].reshape(CHANNELS, -1)
            weight_sum = weight_sum + lax.dot_general(stacked, flat_input, (((1,), (1,)), ((), ())), preferred_element_type=jnp.float32)
            bias_sum = bias_sum + lax.optimization_barrier(jnp.sum(slope_grad.astype(jnp.float32), axis=(1, 2, 3)))
            input_grad = lax.dot_general(weight_rows, stacked, (((0,), (0,)), ((), ())), preferred_element_type=jnp.float32)
            downstream.append(input_grad.reshape(slope_grad.shape).astype(jnp.bfloat16))
        upstream = jnp.stack(downstream)
        weight_grads.append((weight_sum * norm_scale).reshape(CHANNELS, 27, CHANNELS))
        bias_grads.append(bias_sum * norm_scale)
        input_grads.append(upstream)
    return (jnp.stack(weight_grads[::-1]), jnp.stack(bias_grads[::-1]), jnp.stack(input_grads[::-1]))
```

```python
import math

import jax
import jax.numpy as jnp
from jax import lax
from jax.sharding import PartitionSpec as P

CHUNK = 1

PAD3 = ((1, 1), (1, 1), (1, 1))


def silu_slope(pre_act):
    sigmoid = jax.nn.sigmoid(pre_act)
    return sigmoid * (1.0 + pre_act * (1.0 - sigmoid))


def conv_forward(act, kernel):
    return lax.conv_general_dilated(
        act, kernel, (1, 1, 1), PAD3,
        dimension_numbers=("NCDHW", "ODHWI", "NCDHW"),
        preferred_element_type=jnp.float32,
    )


def conv_input_grad(slope, kernel):
    flipped = kernel[:, ::-1, ::-1, ::-1, :]
    return lax.conv_general_dilated(
        slope, flipped, (1, 1, 1), PAD3,
        dimension_numbers=("NCDHW", "IDHWO", "NCDHW"),
        preferred_element_type=jnp.float32,
    )


def conv_weight_grad(act, slope):
    return lax.conv_general_dilated(
        act, slope, (1, 1, 1), PAD3,
        dimension_numbers=("CNDHW", "IODHW", "CDHWN"),
        preferred_element_type=jnp.float32,
    )


def local(volumes, weights, biases, cotangent):
    section_count = lax.axis_size("section")
    section_pos = lax.axis_index("section")
    micro_count = volumes.shape[0]
    chunk = CHUNK if micro_count % CHUNK == 0 else 1
    chunk_count = micro_count // chunk
    tick_count = chunk_count + section_count - 1
    own_count, tap_count, channels = weights.shape[1:]
    extent = volumes.shape[2:]
    kernel = weights[0].reshape(own_count, 3, 3, 3, channels)
    layer_bias = biases[0][None, :, None, None, None]
    slab = (chunk, own_count) + tuple(extent)
    forward_pairs = [(i, i + 1) for i in range(section_count - 1)]
    backward_pairs = [(i + 1, i) for i in range(section_count - 1)]

    incoming = jnp.zeros(slab, jnp.bfloat16)
    gathered = []
    pres = []
    for tick in range(tick_count):
        if tick < chunk_count:
            first = volumes[tick * chunk:(tick + 1) * chunk]
        else:
            first = jnp.zeros(slab, jnp.bfloat16)
        own_input = jnp.where(section_pos == 0, first, incoming)
        full_input = lax.all_gather(own_input, "filt", axis=1, tiled=True)
        pre_act = conv_forward(full_input, kernel) + layer_bias
        gathered.append(full_input)
        pres.append(pre_act)
        if tick < tick_count - 1:
            outgoing = jax.nn.silu(pre_act).astype(jnp.bfloat16)
            incoming = lax.ppermute(outgoing, "section", forward_pairs)

    incoming = jnp.zeros(slab, jnp.bfloat16)
    grad_kernel = jnp.zeros((own_count, 3, 3, 3, channels), jnp.float32)
    grad_bias = jnp.zeros((own_count,), jnp.float32)
    results = []
    for tick in range(tick_count):
        forward_tick = tick_count - 1 - tick
        if tick < chunk_count:
            start = (chunk_count - 1 - tick) * chunk
            last = cotangent[start:start + chunk]
        else:
            last = jnp.zeros(slab, jnp.bfloat16)
        upstream = jnp.where(section_pos == section_count - 1, last, incoming)
        sample = forward_tick - section_pos
        in_range = (sample >= 0) & (sample < chunk_count)
        slope = (upstream.astype(jnp.float32) * silu_slope(pres[forward_tick])).astype(jnp.bfloat16)
        slope = jnp.where(in_range, slope, jnp.zeros((), jnp.bfloat16))
        grad_kernel = grad_kernel + conv_weight_grad(gathered[forward_tick], slope)
        grad_bias = grad_bias + jnp.sum(slope.astype(jnp.float32), axis=(0, 2, 3, 4))
        partial = jnp.moveaxis(conv_input_grad(slope, kernel).astype(jnp.bfloat16), 1, 0)
        partial = partial.reshape(channels, chunk * extent[0] * extent[1], extent[2])
        scattered = lax.psum_scatter(partial, "filt", scatter_dimension=0, tiled=True)
        input_grad = jnp.moveaxis(scattered.reshape((own_count, chunk) + tuple(extent)), 0, 1)
        results.append(input_grad)
        if tick < tick_count - 1:
            incoming = lax.ppermute(input_grad, "section", backward_pairs)

    reversed_results = jnp.stack(results[::-1])
    picked = lax.dynamic_slice_in_dim(reversed_results, section_pos, chunk_count, axis=0)
    grad_in = picked.reshape((1, micro_count, own_count) + tuple(extent))
    norm_scale = 1.0 / math.sqrt(micro_count * math.prod(extent))
    return (
        (grad_kernel * norm_scale).reshape(1, own_count, tap_count, channels),
        (grad_bias * norm_scale)[None],
        grad_in,
    )


def solution(mesh):
    in_specs = (
        P("groups", "filt", None, None, None),
        P("section", "filt", None, None),
        P("section", "filt"),
        P("groups", "filt", None, None, None),
    )
    out_specs = (
        P(("groups", "section"), "filt", None, None),
        P(("groups", "section"), "filt"),
        P(("groups", "section"), None, "filt", None, None, None),
    )
    return jax.shard_map(local, mesh=mesh, in_specs=in_specs, out_specs=out_specs, check_vma=False)
```

```python
import functools
import math

import jax
import jax.numpy as jnp
from jax import lax
from jax.experimental import pallas as pl
from jax.experimental.pallas import tpu as pltpu
from jax.sharding import PartitionSpec as P

CHUNK = 1


def lane_shift(values, step, row_len):
    if step == 0:
        return values
    width = values.shape[-1]
    wide = values.astype(jnp.float32)
    rolled = pltpu.roll(wide, (-step) % width, 1)
    z = lax.broadcasted_iota(jnp.int32, values.shape, 1) % row_len
    keep = (z + step >= 0) & (z + step < row_len)
    return jnp.where(keep, rolled, 0.0).astype(values.dtype)


def block_source(block, step_x, step_y, extent_x, extent_y):
    pos_x, pos_y = block // extent_y + step_x, block % extent_y + step_y
    if 0 <= pos_x < extent_x and 0 <= pos_y < extent_y:
        return pos_x * extent_y + pos_y
    return None


def forward_kernel(extent, chunk, act_ref, w_ref, b_ref, out_ref):
    extent_x, extent_y, row_len = extent
    blocks = extent_x * extent_y
    cells = blocks * row_len
    own = out_ref.shape[0]
    for n in range(chunk):
        act = act_ref[:, n * cells:(n + 1) * cells]
        acc = [None] * blocks
        for c_index, step_z in enumerate((-1, 0, 1)):
            shifted = lane_shift(act, step_z, row_len)
            product = jnp.dot(w_ref[c_index], shifted, preferred_element_type=jnp.float32)
            for a_index, step_x in enumerate((-1, 0, 1)):
                for b_index, step_y in enumerate((-1, 0, 1)):
                    rows = (a_index * 3 + b_index) * own
                    for block in range(blocks):
                        src = block_source(block, step_x, step_y, extent_x, extent_y)
                        if src is None:
                            continue
                        piece = product[rows:rows + own, src * row_len:(src + 1) * row_len]
                        acc[block] = piece if acc[block] is None else acc[block] + piece
        total = jnp.concatenate(acc, axis=1) + b_ref[...]
        out_ref[:, n * cells:(n + 1) * cells] = total


def backward_kernel(extent, chunk, slope_ref, act_ref, w_ref, acc_ref, gin_ref, gw_ref, stack_ref):
    extent_x, extent_y, row_len = extent
    blocks = extent_x * extent_y
    cells = blocks * row_len
    own = slope_ref.shape[0]
    gw = acc_ref[...]
    zero_block = jnp.zeros((own, row_len), stack_ref.dtype)
    for n in range(chunk):
        slope = slope_ref[:, n * cells:(n + 1) * cells]
        for c_index, step_z in enumerate((-1, 0, 1)):
            shifted = lane_shift(slope, -step_z, row_len)
            for a_index, step_x in enumerate((-1, 0, 1)):
                for b_index, step_y in enumerate((-1, 0, 1)):
                    tap = a_index * 9 + b_index * 3 + c_index
                    pieces = []
                    for block in range(blocks):
                        src = block_source(block, -step_x, -step_y, extent_x, extent_y)
                        if src is None:
                            pieces.append(zero_block)
                        else:
                            pieces.append(shifted[:, src * row_len:(src + 1) * row_len])
                    stack_ref[tap * own:(tap + 1) * own, :] = jnp.concatenate(pieces, axis=1)
        stacked = stack_ref[...]
        gin_ref[:, n * cells:(n + 1) * cells] = jnp.dot(
            w_ref[...], stacked, preferred_element_type=jnp.float32
        ).astype(gin_ref.dtype)
        gw = gw + lax.dot_general(
            stacked, act_ref[:, n * cells:(n + 1) * cells], (((1,), (1,)), ((), ())),
            preferred_element_type=jnp.float32,
        )
    gw_ref[...] = gw


def conv_forward_call(act, w_fwd, bias_col, extent, chunk):
    own = bias_col.shape[0]
    return pl.pallas_call(
        functools.partial(forward_kernel, extent, chunk),
        out_shape=jax.ShapeDtypeStruct((own, act.shape[1]), jnp.float32),
        compiler_params=pltpu.CompilerParams(vmem_limit_bytes=48 * 1024 * 1024),
    )(act, w_fwd, bias_col)


def conv_backward_call(slope, act, w_bwd, acc, extent, chunk):
    own = slope.shape[0]
    channels = act.shape[0]
    cells = extent[0] * extent[1] * extent[2]
    return pl.pallas_call(
        functools.partial(backward_kernel, extent, chunk),
        out_shape=(
            jax.ShapeDtypeStruct((channels, act.shape[1]), jnp.bfloat16),
            jax.ShapeDtypeStruct(acc.shape, jnp.float32),
        ),
        scratch_shapes=[pltpu.VMEM((27 * own, cells), jnp.bfloat16)],
        input_output_aliases={3: 1},
        compiler_params=pltpu.CompilerParams(vmem_limit_bytes=48 * 1024 * 1024),
    )(slope, act, w_bwd, acc)

def take_blocks(values, axis, order):
    count = order.shape[0]
    shape = values.shape
    split = shape[:axis] + (count, shape[axis] // count) + shape[axis + 1:]
    picked = jnp.take(values.reshape(split), order, axis=axis)
    return picked.reshape(shape)


RING_LIMIT = 4


def ring_gather(value, count):
    if count > RING_LIMIT:
        return lax.all_gather(value, "filt", axis=0, tiled=True)
    pieces = [value]
    for step in range(1, count):
        pieces.append(lax.ppermute(value, "filt", [(j, (j + step) % count) for j in range(count)]))
    return jnp.concatenate(pieces, axis=0)


def ring_scatter_sum(partial, count):
    if count > RING_LIMIT:
        return lax.psum_scatter(partial, "filt", scatter_dimension=0, tiled=True)
    rows = partial.shape[0] // count
    total = partial[:rows].astype(jnp.float32)
    for step in range(1, count):
        piece = partial[step * rows:(step + 1) * rows].astype(jnp.bfloat16)
        total = total + lax.ppermute(
            piece, "filt", [(j, (j + step) % count) for j in range(count)]
        ).astype(jnp.float32)
    return total.astype(jnp.bfloat16)


def silu_slope(pre_act):
    sigmoid = jax.nn.sigmoid(pre_act)
    return sigmoid * (1.0 + pre_act * (1.0 - sigmoid))


def local(volumes, weights, biases, cotangent):
    section_count = lax.axis_size("section")
    section_pos = lax.axis_index("section")
    micro_count = volumes.shape[0]
    chunk = CHUNK if micro_count % CHUNK == 0 else 1
    chunk_count = micro_count // chunk
    tick_count = chunk_count + section_count - 1
    own_count, tap_count, channels = weights.shape[1:]
    extent = tuple(volumes.shape[2:])
    cells = extent[0] * extent[1] * extent[2]
    width = chunk * cells
    weight = weights[0]
    w_fwd = jnp.transpose(weight.reshape(own_count, 3, 3, 3, channels), (3, 1, 2, 0, 4)).reshape(
        3, 9 * own_count, channels
    )
    w_bwd = jnp.transpose(weight, (2, 1, 0)).reshape(channels, tap_count * own_count)
    filt_count = lax.axis_size("filt")
    filt_pos = lax.axis_index("filt")
    if filt_count > RING_LIMIT:
        back_order = jnp.arange(filt_count)
        ahead_order = jnp.arange(filt_count)
    else:
        back_order = (filt_pos - jnp.arange(filt_count)) % filt_count
        ahead_order = (filt_pos + jnp.arange(filt_count)) % filt_count
    w_fwd = take_blocks(w_fwd, 2, back_order)
    w_bwd = take_blocks(w_bwd, 0, ahead_order)
    bias_col = biases[0][:, None]
    flat_volumes = jnp.transpose(volumes.reshape(micro_count, own_count, cells), (1, 0, 2)).reshape(
        own_count, micro_count * cells
    )
    flat_cotangent = jnp.transpose(
        cotangent.reshape(micro_count, own_count, cells), (1, 0, 2)
    ).reshape(own_count, micro_count * cells)
    slab = (own_count, width)
    forward_pairs = [(i, i + 1) for i in range(section_count - 1)]
    backward_pairs = [(i + 1, i) for i in range(section_count - 1)]

    incoming = jnp.zeros(slab, jnp.bfloat16)
    gathered = []
    pres = []
    for tick in range(tick_count):
        if tick < chunk_count:
            first = flat_volumes[:, tick * width:(tick + 1) * width]
        else:
            first = jnp.zeros(slab, jnp.bfloat16)
        own_input = jnp.where(section_pos == 0, first, incoming)
        full_input = ring_gather(own_input, filt_count)
        pre_act = conv_forward_call(full_input, w_fwd, bias_col, extent, chunk)
        gathered.append(full_input)
        pres.append(pre_act)
        if tick < tick_count - 1:
            outgoing = jax.nn.silu(pre_act).astype(jnp.bfloat16)
            incoming = lax.ppermute(outgoing, "section", forward_pairs)

    incoming = jnp.zeros(slab, jnp.bfloat16)
    grad_rows = jnp.zeros((tap_count * own_count, channels), jnp.float32)
    grad_bias = jnp.zeros((own_count,), jnp.float32)
    results = []
    for tick in range(tick_count):
        forward_tick = tick_count - 1 - tick
        if tick < chunk_count:
            start = (chunk_count - 1 - tick) * width
            last = flat_cotangent[:, start:start + width]
        else:
            last = jnp.zeros(slab, jnp.bfloat16)
        upstream = jnp.where(section_pos == section_count - 1, last, incoming)
        sample = forward_tick - section_pos
        in_range = (sample >= 0) & (sample < chunk_count)
        slope = (upstream.astype(jnp.float32) * silu_slope(pres[forward_tick])).astype(jnp.bfloat16)
        slope = jnp.where(in_range, slope, jnp.zeros((), jnp.bfloat16))
        grad_bias = grad_bias + jnp.sum(slope.astype(jnp.float32), axis=1)
        partial, grad_rows = conv_backward_call(
            slope, gathered[forward_tick], w_bwd, grad_rows, extent, chunk
        )
        input_grad = ring_scatter_sum(partial, filt_count)
        results.append(input_grad)
        if tick < tick_count - 1:
            incoming = lax.ppermute(input_grad, "section", backward_pairs)

    stacked_results = jnp.stack(results[::-1]).reshape(tick_count, own_count, chunk, cells)
    stacked_results = jnp.transpose(stacked_results, (0, 2, 1, 3))
    picked = lax.dynamic_slice_in_dim(stacked_results, section_pos, chunk_count, axis=0)
    grad_in = picked.reshape((1, micro_count, own_count) + extent)
    norm_scale = 1.0 / math.sqrt(micro_count * cells)
    grad_rows = take_blocks(grad_rows, 1, back_order)
    grad_kernel = jnp.transpose(grad_rows.reshape(tap_count, own_count, channels), (1, 0, 2))
    return (
        (grad_kernel * norm_scale)[None],
        (grad_bias * norm_scale)[None],
        grad_in,
    )


def solution(mesh):
    in_specs = (
        P("groups", "filt", None, None, None),
        P("section", "filt", None, None),
        P("section", "filt"),
        P("groups", "filt", None, None, None),
    )
    out_specs = (
        P(("groups", "section"), "filt", None, None),
        P(("groups", "section"), "filt"),
        P(("groups", "section"), None, "filt", None, None, None),
    )
    return jax.shard_map(local, mesh=mesh, in_specs=in_specs, out_specs=out_specs, check_vma=False)
```

```python
import functools
import math

import jax
import jax.numpy as jnp
from jax import lax
from jax.experimental import pallas as pl
from jax.experimental.pallas import tpu as pltpu
from jax.sharding import PartitionSpec as P

CHUNK = 1


def lane_shift(values, step, row_len):
    if step == 0:
        return values
    width = values.shape[-1]
    wide = values.astype(jnp.float32)
    rolled = pltpu.roll(wide, (-step) % width, 1)
    z = lax.broadcasted_iota(jnp.int32, values.shape, 1) % row_len
    keep = (z + step >= 0) & (z + step < row_len)
    return jnp.where(keep, rolled, 0.0).astype(values.dtype)


def block_source(block, step_x, step_y, extent_x, extent_y):
    pos_x, pos_y = block // extent_y + step_x, block % extent_y + step_y
    if 0 <= pos_x < extent_x and 0 <= pos_y < extent_y:
        return pos_x * extent_y + pos_y
    return None


def forward_kernel(extent, chunk, act_ref, w_ref, b_ref, out_ref):
    extent_x, extent_y, row_len = extent
    blocks = extent_x * extent_y
    cells = blocks * row_len
    own = out_ref.shape[0]
    for n in range(chunk):
        act = act_ref[:, n * cells:(n + 1) * cells]
        acc = [None] * blocks
        for c_index, step_z in enumerate((-1, 0, 1)):
            shifted = lane_shift(act, step_z, row_len)
            product = jnp.dot(w_ref[c_index], shifted, preferred_element_type=jnp.float32)
            for a_index, step_x in enumerate((-1, 0, 1)):
                for b_index, step_y in enumerate((-1, 0, 1)):
                    rows = (a_index * 3 + b_index) * own
                    for block in range(blocks):
                        src = block_source(block, step_x, step_y, extent_x, extent_y)
                        if src is None:
                            continue
                        piece = product[rows:rows + own, src * row_len:(src + 1) * row_len]
                        acc[block] = piece if acc[block] is None else acc[block] + piece
        total = jnp.concatenate(acc, axis=1) + b_ref[...]
        out_ref[:, n * cells:(n + 1) * cells] = total


def build_stack(extent, slope, stack_ref):
    extent_x, extent_y, row_len = extent
    blocks = extent_x * extent_y
    own = slope.shape[0]
    zero_block = jnp.zeros((own, row_len), stack_ref.dtype)
    for c_index, step_z in enumerate((-1, 0, 1)):
        shifted = lane_shift(slope, -step_z, row_len)
        for a_index, step_x in enumerate((-1, 0, 1)):
            for b_index, step_y in enumerate((-1, 0, 1)):
                tap = a_index * 9 + b_index * 3 + c_index
                pieces = []
                for block in range(blocks):
                    src = block_source(block, -step_x, -step_y, extent_x, extent_y)
                    if src is None:
                        pieces.append(zero_block)
                    else:
                        pieces.append(shifted[:, src * row_len:(src + 1) * row_len])
                stack_ref[tap * own:(tap + 1) * own, :] = jnp.concatenate(pieces, axis=1)


def input_grad_kernel(extent, chunk, slope_ref, w_ref, bias_acc_ref, gin_ref, gb_ref, stack_ref):
    cells = extent[0] * extent[1] * extent[2]
    gb = bias_acc_ref[...]
    for n in range(chunk):
        slope = slope_ref[:, n * cells:(n + 1) * cells]
        gb = gb + jnp.sum(slope.astype(jnp.float32), axis=1, keepdims=True)
        build_stack(extent, slope, stack_ref)
        gin_ref[:, n * cells:(n + 1) * cells] = jnp.dot(
            w_ref[...], stack_ref[...], preferred_element_type=jnp.float32
        ).astype(gin_ref.dtype)
    gb_ref[...] = gb


def weight_grad_kernel(extent, chunk, slope_ref, act_ref, acc_ref, gw_ref, stack_ref):
    cells = extent[0] * extent[1] * extent[2]
    gw = acc_ref[...]
    for n in range(chunk):
        build_stack(extent, slope_ref[:, n * cells:(n + 1) * cells], stack_ref)
        gw = gw + lax.dot_general(
            stack_ref[...], act_ref[:, n * cells:(n + 1) * cells], (((1,), (1,)), ((), ())),
            preferred_element_type=jnp.float32,
        )
    gw_ref[...] = gw


def conv_forward_call(act, w_fwd, bias_col, extent, chunk):
    own = bias_col.shape[0]
    return pl.pallas_call(
        functools.partial(forward_kernel, extent, chunk),
        out_shape=jax.ShapeDtypeStruct((own, act.shape[1]), jnp.float32),
        compiler_params=pltpu.CompilerParams(vmem_limit_bytes=48 * 1024 * 1024),
    )(act, w_fwd, bias_col)


def conv_backward_call(slope, act, w_bwd, acc, bias_acc, extent, chunk):
    own = slope.shape[0]
    channels = act.shape[0]
    cells = extent[0] * extent[1] * extent[2]
    params = pltpu.CompilerParams(vmem_limit_bytes=48 * 1024 * 1024)
    gin, gb = pl.pallas_call(
        functools.partial(input_grad_kernel, extent, chunk),
        out_shape=(
            jax.ShapeDtypeStruct((channels, act.shape[1]), jnp.bfloat16),
            jax.ShapeDtypeStruct(bias_acc.shape, jnp.float32),
        ),
        scratch_shapes=[pltpu.VMEM((27 * own, cells), jnp.bfloat16)],
        input_output_aliases={2: 1},
        compiler_params=params,
    )(slope, w_bwd, bias_acc)
    gw = pl.pallas_call(
        functools.partial(weight_grad_kernel, extent, chunk),
        out_shape=jax.ShapeDtypeStruct(acc.shape, jnp.float32),
        scratch_shapes=[pltpu.VMEM((27 * own, cells), jnp.bfloat16)],
        input_output_aliases={2: 0},
        compiler_params=params,
    )(slope, act, acc)
    return gin, gw, gb


def take_blocks(values, axis, order):
    count = order.shape[0]
    shape = values.shape
    split = shape[:axis] + (count, shape[axis] // count) + shape[axis + 1:]
    picked = jnp.take(values.reshape(split), order, axis=axis)
    return picked.reshape(shape)


RING_LIMIT = 4


def step_order(count):
    steps = list(range(1, count))
    middle = count // 2
    return [middle] + [step for step in steps if step != middle]


def ring_gather(value, count):
    if count > RING_LIMIT:
        return lax.all_gather(value, "filt", axis=0, tiled=True)
    pieces = {0: value}
    for step in step_order(count):
        pieces[step] = lax.ppermute(value, "filt", [(j, (j + step) % count) for j in range(count)])
    return jnp.concatenate([pieces[step] for step in range(count)], axis=0)


def ring_scatter_sum(partial, count):
    if count > RING_LIMIT:
        return lax.psum_scatter(partial, "filt", scatter_dimension=0, tiled=True)
    rows = partial.shape[0] // count
    total = partial[:rows].astype(jnp.float32)
    for step in step_order(count):
        piece = partial[step * rows:(step + 1) * rows].astype(jnp.bfloat16)
        total = total + lax.ppermute(
            piece, "filt", [(j, (j + step) % count) for j in range(count)]
        ).astype(jnp.float32)
    return total.astype(jnp.bfloat16)


def silu_slope(pre_act):
    sigmoid = jax.nn.sigmoid(pre_act)
    return sigmoid * (1.0 + pre_act * (1.0 - sigmoid))


def local(volumes, weights, biases, cotangent):
    section_count = lax.axis_size("section")
    section_pos = lax.axis_index("section")
    micro_count = volumes.shape[0]
    chunk = CHUNK if micro_count % CHUNK == 0 else 1
    chunk_count = micro_count // chunk
    tick_count = chunk_count + section_count - 1
    own_count, tap_count, channels = weights.shape[1:]
    extent = tuple(volumes.shape[2:])
    cells = extent[0] * extent[1] * extent[2]
    width = chunk * cells
    weight = weights[0]
    w_fwd = jnp.transpose(weight.reshape(own_count, 3, 3, 3, channels), (3, 1, 2, 0, 4)).reshape(
        3, 9 * own_count, channels
    )
    w_bwd = jnp.transpose(weight, (2, 1, 0)).reshape(channels, tap_count * own_count)
    filt_count = lax.axis_size("filt")
    filt_pos = lax.axis_index("filt")
    if filt_count > RING_LIMIT:
        back_order = jnp.arange(filt_count)
        ahead_order = jnp.arange(filt_count)
    else:
        back_order = (filt_pos - jnp.arange(filt_count)) % filt_count
        ahead_order = (filt_pos + jnp.arange(filt_count)) % filt_count
    w_fwd = take_blocks(w_fwd, 2, back_order)
    w_bwd = take_blocks(w_bwd, 0, ahead_order)
    bias_col = biases[0][:, None]
    flat_volumes = jnp.transpose(volumes.reshape(micro_count, own_count, cells), (1, 0, 2)).reshape(
        own_count, micro_count * cells
    )
    flat_cotangent = jnp.transpose(
        cotangent.reshape(micro_count, own_count, cells), (1, 0, 2)
    ).reshape(own_count, micro_count * cells)
    slab = (own_count, width)
    forward_pairs = [(i, i + 1) for i in range(section_count - 1)]
    backward_pairs = [(i + 1, i) for i in range(section_count - 1)]

    incoming = jnp.zeros(slab, jnp.bfloat16)
    gathered = []
    pres = []
    for tick in range(tick_count):
        if tick < chunk_count:
            first = flat_volumes[:, tick * width:(tick + 1) * width]
        else:
            first = jnp.zeros(slab, jnp.bfloat16)
        own_input = jnp.where(section_pos == 0, first, incoming)
        full_input = ring_gather(own_input, filt_count)
        pre_act = conv_forward_call(full_input, w_fwd, bias_col, extent, chunk)
        gathered.append(full_input)
        pres.append(pre_act)
        if tick < tick_count - 1:
            outgoing = jax.nn.silu(pre_act).astype(jnp.bfloat16)
            incoming = lax.ppermute(outgoing, "section", forward_pairs)

    incoming = jnp.zeros(slab, jnp.bfloat16)
    grad_rows = jnp.zeros((tap_count * own_count, channels), jnp.float32)
    grad_bias = jnp.zeros((own_count, 1), jnp.float32)
    results = []
    for tick in range(tick_count):
        forward_tick = tick_count - 1 - tick
        if tick < chunk_count:
            start = (chunk_count - 1 - tick) * width
            last = flat_cotangent[:, start:start + width]
        else:
            last = jnp.zeros(slab, jnp.bfloat16)
        upstream = jnp.where(section_pos == section_count - 1, last, incoming)
        sample = forward_tick - section_pos
        in_range = (sample >= 0) & (sample < chunk_count)
        slope = (upstream.astype(jnp.float32) * silu_slope(pres[forward_tick])).astype(jnp.bfloat16)
        slope = jnp.where(in_range, slope, jnp.zeros((), jnp.bfloat16))
        partial, grad_rows, grad_bias = conv_backward_call(
            slope, gathered[forward_tick], w_bwd, grad_rows, grad_bias, extent, chunk
        )
        input_grad = ring_scatter_sum(partial, filt_count)
        results.append(input_grad)
        if tick < tick_count - 1:
            incoming = lax.ppermute(input_grad, "section", backward_pairs)

    stacked_results = jnp.stack(results[::-1]).reshape(tick_count, own_count, chunk, cells)
    stacked_results = jnp.transpose(stacked_results, (0, 2, 1, 3))
    picked = lax.dynamic_slice_in_dim(stacked_results, section_pos, chunk_count, axis=0)
    grad_in = picked.reshape((1, micro_count, own_count) + extent)
    norm_scale = 1.0 / math.sqrt(micro_count * cells)
    grad_rows = take_blocks(grad_rows, 1, back_order)
    grad_kernel = jnp.transpose(grad_rows.reshape(tap_count, own_count, channels), (1, 0, 2))
    return (
        (grad_kernel * norm_scale)[None],
        (grad_bias[:, 0] * norm_scale)[None],
        grad_in,
    )


def solution(mesh):
    in_specs = (
        P("groups", "filt", None, None, None),
        P("section", "filt", None, None),
        P("section", "filt"),
        P("groups", "filt", None, None, None),
    )
    out_specs = (
        P(("groups", "section"), "filt", None, None),
        P(("groups", "section"), "filt"),
        P(("groups", "section"), None, "filt", None, None, None),
    )
    return jax.shard_map(local, mesh=mesh, in_specs=in_specs, out_specs=out_specs, check_vma=False)
```

```python
import functools
import math

import jax
import jax.numpy as jnp
from jax import lax
from jax.experimental import pallas as pl
from jax.experimental.pallas import tpu as pltpu
from jax.sharding import PartitionSpec as P

CHUNK = 1


def lane_shift(values, step, row_len):
    if step == 0:
        return values
    width = values.shape[-1]
    wide = values.astype(jnp.float32)
    rolled = pltpu.roll(wide, (-step) % width, 1)
    z = lax.broadcasted_iota(jnp.int32, values.shape, 1) % row_len
    keep = (z + step >= 0) & (z + step < row_len)
    return jnp.where(keep, rolled, 0.0).astype(values.dtype)


def block_source(block, step_x, step_y, extent_x, extent_y):
    pos_x, pos_y = block // extent_y + step_x, block % extent_y + step_y
    if 0 <= pos_x < extent_x and 0 <= pos_y < extent_y:
        return pos_x * extent_y + pos_y
    return None


def forward_kernel(extent, chunk, act_ref, w_ref, b_ref, out_ref):
    extent_x, extent_y, row_len = extent
    blocks = extent_x * extent_y
    cells = blocks * row_len
    own = out_ref.shape[0]
    for n in range(chunk):
        act = act_ref[:, n * cells:(n + 1) * cells]
        acc = [None] * blocks
        for c_index, step_z in enumerate((-1, 0, 1)):
            shifted = lane_shift(act, step_z, row_len)
            product = jnp.dot(w_ref[c_index], shifted, preferred_element_type=jnp.float32)
            for a_index, step_x in enumerate((-1, 0, 1)):
                for b_index, step_y in enumerate((-1, 0, 1)):
                    rows = (a_index * 3 + b_index) * own
                    for block in range(blocks):
                        src = block_source(block, step_x, step_y, extent_x, extent_y)
                        if src is None:
                            continue
                        piece = product[rows:rows + own, src * row_len:(src + 1) * row_len]
                        acc[block] = piece if acc[block] is None else acc[block] + piece
        total = jnp.concatenate(acc, axis=1) + b_ref[...]
        out_ref[:, n * cells:(n + 1) * cells] = total


def build_stack(extent, slope, stack_ref):
    extent_x, extent_y, row_len = extent
    blocks = extent_x * extent_y
    own = slope.shape[0]
    zero_block = jnp.zeros((own, row_len), stack_ref.dtype)
    for c_index, step_z in enumerate((-1, 0, 1)):
        shifted = lane_shift(slope, -step_z, row_len)
        for a_index, step_x in enumerate((-1, 0, 1)):
            for b_index, step_y in enumerate((-1, 0, 1)):
                tap = a_index * 9 + b_index * 3 + c_index
                pieces = []
                for block in range(blocks):
                    src = block_source(block, -step_x, -step_y, extent_x, extent_y)
                    if src is None:
                        pieces.append(zero_block)
                    else:
                        pieces.append(shifted[:, src * row_len:(src + 1) * row_len])
                stack_ref[tap * own:(tap + 1) * own, :] = jnp.concatenate(pieces, axis=1)


def input_grad_kernel(extent, chunk, slope_ref, w_ref, bias_acc_ref, gin_ref, gb_ref, stack_ref):
    cells = extent[0] * extent[1] * extent[2]
    gb = bias_acc_ref[...]
    for n in range(chunk):
        slope = slope_ref[:, n * cells:(n + 1) * cells]
        gb = gb + jnp.sum(slope.astype(jnp.float32), axis=1, keepdims=True)
        build_stack(extent, slope, stack_ref)
        gin_ref[:, n * cells:(n + 1) * cells] = jnp.dot(
            w_ref[...], stack_ref[...], preferred_element_type=jnp.float32
        ).astype(gin_ref.dtype)
    gb_ref[...] = gb


def weight_grad_kernel(extent, chunk, slope_ref, act_ref, acc_ref, gw_ref, stack_ref):
    cells = extent[0] * extent[1] * extent[2]
    gw = acc_ref[...]
    for n in range(chunk):
        build_stack(extent, slope_ref[:, n * cells:(n + 1) * cells], stack_ref)
        gw = gw + lax.dot_general(
            stack_ref[...], act_ref[:, n * cells:(n + 1) * cells], (((1,), (1,)), ((), ())),
            preferred_element_type=jnp.float32,
        )
    gw_ref[...] = gw


def conv_forward_call(act, w_fwd, bias_col, extent, chunk):
    own = bias_col.shape[0]
    return pl.pallas_call(
        functools.partial(forward_kernel, extent, chunk),
        out_shape=jax.ShapeDtypeStruct((own, act.shape[1]), jnp.float32),
        compiler_params=pltpu.CompilerParams(vmem_limit_bytes=48 * 1024 * 1024),
    )(act, w_fwd, bias_col)


def conv_backward_call(slope, act, w_bwd, acc, bias_acc, extent, chunk):
    own = slope.shape[0]
    channels = act.shape[0]
    cells = extent[0] * extent[1] * extent[2]
    params = pltpu.CompilerParams(vmem_limit_bytes=48 * 1024 * 1024)
    gin, gb = pl.pallas_call(
        functools.partial(input_grad_kernel, extent, chunk),
        out_shape=(
            jax.ShapeDtypeStruct((channels, act.shape[1]), jnp.bfloat16),
            jax.ShapeDtypeStruct(bias_acc.shape, jnp.float32),
        ),
        scratch_shapes=[pltpu.VMEM((27 * own, cells), jnp.bfloat16)],
        input_output_aliases={2: 1},
        compiler_params=params,
    )(slope, w_bwd, bias_acc)
    gw = pl.pallas_call(
        functools.partial(weight_grad_kernel, extent, chunk),
        out_shape=jax.ShapeDtypeStruct(acc.shape, jnp.float32),
        scratch_shapes=[pltpu.VMEM((27 * own, cells), jnp.bfloat16)],
        input_output_aliases={2: 0},
        compiler_params=params,
    )(slope, act, acc)
    return gin, gw, gb


def take_blocks(values, axis, order):
    count = order.shape[0]
    shape = values.shape
    split = shape[:axis] + (count, shape[axis] // count) + shape[axis + 1:]
    picked = jnp.take(values.reshape(split), order, axis=axis)
    return picked.reshape(shape)


RING_LIMIT = 4


def step_order(count):
    steps = list(range(1, count))
    middle = count // 2
    return [middle] + [step for step in steps if step != middle]


def ring_gather(value, count):
    if count > RING_LIMIT:
        return lax.all_gather(value, "filt", axis=0, tiled=True)
    pieces = {0: value}
    for step in step_order(count):
        pieces[step] = lax.ppermute(value, "filt", [(j, (j + step) % count) for j in range(count)])
    return jnp.concatenate([pieces[step] for step in range(count)], axis=0)


def ring_scatter_sum(partial, count):
    if count > RING_LIMIT:
        return lax.psum_scatter(partial, "filt", scatter_dimension=0, tiled=True)
    rows = partial.shape[0] // count
    total = partial[:rows].astype(jnp.float32)
    for step in step_order(count):
        piece = partial[step * rows:(step + 1) * rows].astype(jnp.bfloat16)
        total = total + lax.ppermute(
            piece, "filt", [(j, (j + step) % count) for j in range(count)]
        ).astype(jnp.float32)
    return total.astype(jnp.bfloat16)


def crop_columns(values, first, chunk, own_count, cells):
    pieces = [values[first + n].reshape(own_count, cells) for n in range(chunk)]
    return pieces[0] if chunk == 1 else jnp.concatenate(pieces, axis=1)


def silu_slope(pre_act):
    sigmoid = jax.nn.sigmoid(pre_act)
    return sigmoid * (1.0 + pre_act * (1.0 - sigmoid))


def local(volumes, weights, biases, cotangent):
    section_count = lax.axis_size("section")
    section_pos = lax.axis_index("section")
    micro_count = volumes.shape[0]
    chunk = CHUNK if micro_count % CHUNK == 0 else 1
    chunk_count = micro_count // chunk
    tick_count = chunk_count + section_count - 1
    own_count, tap_count, channels = weights.shape[1:]
    extent = tuple(volumes.shape[2:])
    cells = extent[0] * extent[1] * extent[2]
    width = chunk * cells
    weight = weights[0]
    w_fwd = jnp.transpose(weight.reshape(own_count, 3, 3, 3, channels), (3, 1, 2, 0, 4)).reshape(
        3, 9 * own_count, channels
    )
    w_bwd = jnp.transpose(weight, (2, 1, 0)).reshape(channels, tap_count * own_count)
    filt_count = lax.axis_size("filt")
    filt_pos = lax.axis_index("filt")
    if filt_count > RING_LIMIT:
        back_order = jnp.arange(filt_count)
        ahead_order = jnp.arange(filt_count)
    else:
        back_order = (filt_pos - jnp.arange(filt_count)) % filt_count
        ahead_order = (filt_pos + jnp.arange(filt_count)) % filt_count
    w_fwd = take_blocks(w_fwd, 2, back_order)
    w_bwd = take_blocks(w_bwd, 0, ahead_order)
    bias_col = biases[0][:, None]
    slab = (own_count, width)
    forward_pairs = [(i, i + 1) for i in range(section_count - 1)]
    backward_pairs = [(i + 1, i) for i in range(section_count - 1)]

    incoming = jnp.zeros(slab, jnp.bfloat16)
    gathered = []
    pres = []
    for tick in range(tick_count):
        if tick < chunk_count:
            first = crop_columns(volumes, tick * chunk, chunk, own_count, cells)
        else:
            first = jnp.zeros(slab, jnp.bfloat16)
        own_input = jnp.where(section_pos == 0, first, incoming)
        full_input = ring_gather(own_input, filt_count)
        pre_act = conv_forward_call(full_input, w_fwd, bias_col, extent, chunk)
        gathered.append(full_input)
        pres.append(pre_act)
        if tick < tick_count - 1:
            outgoing = jax.nn.silu(pre_act).astype(jnp.bfloat16)
            incoming = lax.ppermute(outgoing, "section", forward_pairs)

    incoming = jnp.zeros(slab, jnp.bfloat16)
    grad_rows = jnp.zeros((tap_count * own_count, channels), jnp.float32)
    grad_bias = jnp.zeros((own_count, 1), jnp.float32)
    results = []
    for tick in range(tick_count):
        forward_tick = tick_count - 1 - tick
        if tick < chunk_count:
            start = (chunk_count - 1 - tick) * width
            last = crop_columns(cotangent, start // cells, chunk, own_count, cells)
        else:
            last = jnp.zeros(slab, jnp.bfloat16)
        upstream = jnp.where(section_pos == section_count - 1, last, incoming)
        sample = forward_tick - section_pos
        in_range = (sample >= 0) & (sample < chunk_count)
        slope = (upstream.astype(jnp.float32) * silu_slope(pres[forward_tick])).astype(jnp.bfloat16)
        slope = jnp.where(in_range, slope, jnp.zeros((), jnp.bfloat16))
        partial, grad_rows, grad_bias = conv_backward_call(
            slope, gathered[forward_tick], w_bwd, grad_rows, grad_bias, extent, chunk
        )
        input_grad = ring_scatter_sum(partial, filt_count)
        results.append(input_grad)
        if tick < tick_count - 1:
            incoming = lax.ppermute(input_grad, "section", backward_pairs)

    stacked_results = jnp.stack(results[::-1]).reshape(tick_count, own_count, chunk, cells)
    stacked_results = jnp.transpose(stacked_results, (0, 2, 1, 3))
    picked = lax.dynamic_slice_in_dim(stacked_results, section_pos, chunk_count, axis=0)
    grad_in = picked.reshape((1, micro_count, own_count) + extent)
    norm_scale = 1.0 / math.sqrt(micro_count * cells)
    grad_rows = take_blocks(grad_rows, 1, back_order)
    grad_kernel = jnp.transpose(grad_rows.reshape(tap_count, own_count, channels), (1, 0, 2))
    return (
        (grad_kernel * norm_scale)[None],
        (grad_bias[:, 0] * norm_scale)[None],
        grad_in,
    )


def solution(mesh):
    in_specs = (
        P("groups", "filt", None, None, None),
        P("section", "filt", None, None),
        P("section", "filt"),
        P("groups", "filt", None, None, None),
    )
    out_specs = (
        P(("groups", "section"), "filt", None, None),
        P(("groups", "section"), "filt"),
        P(("groups", "section"), None, "filt", None, None, None),
    )
    return jax.shard_map(local, mesh=mesh, in_specs=in_specs, out_specs=out_specs, check_vma=False)
```
